256 devices in a mesh: row: 8 (over y, core), col: 32 (over x, z).
Axes of the slice: x: 4, y: 4, z: 8, core: 2. Of those that a mesh axis runs over, the one named last changes fastest.
Arguments:
- trailing_adjoint: float32 [12288, 12288], P('row', 'col'), may hold values from -3 to 3, as said below
- panel: float32 [12288, 256], P(('row', 'col')), may hold values from -0.0546875 to 0.0546875
- panel_adjoint: float32 [12288, 256], P(('row', 'col')), may hold values from -6 to 6
- diag_factor: float32 [256, 256], replicated, may hold values from -1 to 2, as said below
- diag_adjoint: float32 [256, 256], P('row', 'col'), may hold values from -6 to 6
Outputs:
- off_adjoint: float32 [12288, 256], P(('row', 'col'))
- block_adjoint: float32 [256, 256], replicated
The draws below stay inside these ranges and needn't reach their ends.
Inputs may be any that keep to these rules, and one draw needn't show every extreme that they name: `trailing_adjoint`: symmetric. `diag_factor`: lower triangular with diagonal entries from 1 to 2.
All inputs are finite; a program needn't handle non-finite values.
Results may differ from the reference program's by a relative error of at most 0.000071.
Values sent between devices are 32-bit elements; how exact they have to be, the bound alone decides.
No kernel may reach another device: no remote copies, remote signals or barrier semaphores. Data moves between devices by JAX's collectives and lax.ppermute only.
A program may use at most 64 MiB of HBM per device.

```python
import math
import jax
import jax.numpy as jnp
from jax import lax

B = 256
N = 12288


def draw_trailing_adjoint(key, part):
    raw = jnp.clip(jax.random.normal(key, (N, N), jnp.float32), -4.0, 4.0)
    return (raw + raw.T) * 0.35


def draw_diag_factor(key, part):
    first = jax.random.fold_in(key, 11)
    second = jax.random.fold_in(key, 23)
    diagonal = jax.random.uniform(first, (B,), jnp.float32, 1.0, 2.0)
    spread = jnp.clip(jax.random.normal(second, (B, B), jnp.float32), -4.0, 4.0)
    lower = jnp.tril(spread, -1) * (0.3 / math.sqrt(B))
    return lower + jnp.diag(diagonal)


def level_of(rng, shape, pieces, least, high):
    factor_of = 1.0
    for position, blocks in pieces:
        heights = jax.random.uniform(jax.random.fold_in(jax.random.fold_in(rng, 6), position), (blocks,), jnp.float32, least / len(pieces), high / len(pieces))
        factor_of = factor_of * jnp.repeat(jnp.exp(heights), shape[position] // blocks).reshape((-1,) + (1,) * (len(shape) - 1 - position))
    return factor_of


def scatter_about(rng, dims, scale, reach, split=(), held_as=jnp.bfloat16):
    level = level_of(rng, dims, split, -0.22, 0.18) if split else 1.0
    values = jax.random.normal(rng, dims, jnp.float32) * scale * level
    return jnp.minimum(jnp.maximum(values, -reach), reach).astype(held_as)


def setup_inputs(seed: int = 0) -> dict:
    arg_keys = jax.random.split(jax.random.key(seed), 6)
    trailing_adjoint = draw_trailing_adjoint(jax.random.fold_in(arg_keys[5], 71), 0)
    panel = scatter_about(arg_keys[1], (N, B), N ** -0.5, 0.0546875, ((0, 256),), jnp.float32)
    panel_adjoint = scatter_about(arg_keys[2], (N, B), 1.0, 6.0, ((0, 256),), jnp.float32)
    diag_factor = draw_diag_factor(jax.random.fold_in(arg_keys[5], 71), 0)
    diag_adjoint = scatter_about(arg_keys[4], (B, B), 1.0, 6.0, ((0, 8), (1, 32)), jnp.float32)
    return {"trailing_adjoint": trailing_adjoint, "panel": panel, "panel_adjoint": panel_adjoint, "diag_factor": diag_factor, "diag_adjoint": diag_adjoint}


def right_solve(factor, rows):
    return jax.scipy.linalg.solve_triangular(factor, rows.T, lower=True, trans=1).T

def left_solve(factor, matrix):
    return jax.scipy.linalg.solve_triangular(factor, matrix, lower=True, trans=1)

def diagonal_adjoint(factor, adjoint):
    product = jnp.dot(factor.T.astype(jnp.float32), adjoint.astype(jnp.float32), precision=lax.Precision.HIGHEST, preferred_element_type=jnp.float32)
    lower = jnp.tril(product) - 0.5 * jnp.diag(jnp.diag(product))
    symmetric = lower + lower.T
    half = left_solve(factor, symmetric)
    return 0.5 * left_solve(factor, half.T).T

def reference(trailing_adjoint, panel, panel_adjoint, diag_factor, diag_adjoint):
    product = jnp.dot(trailing_adjoint.astype(jnp.float32), panel.astype(jnp.float32), precision=lax.Precision.HIGHEST, preferred_element_type=jnp.float32)
    updated = panel_adjoint - 2.0 * product
    off_adjoint = right_solve(diag_factor, updated)
    contribution = jnp.dot(off_adjoint.T.astype(jnp.float32), panel.astype(jnp.float32), precision=lax.Precision.HIGHEST, preferred_element_type=jnp.float32)
    accumulated = diag_adjoint - contribution
    return (off_adjoint, diagonal_adjoint(diag_factor, accumulated))
```

```python
import jax
import jax.numpy as jnp
from jax import lax
from jax.sharding import PartitionSpec as P

ALL = ("row", "col")


def right_solve(factor, rows):
    return jax.scipy.linalg.solve_triangular(factor, rows.T, lower=True, trans=1).T


def left_solve(factor, matrix):
    return jax.scipy.linalg.solve_triangular(factor, matrix, lower=True, trans=1)


def diagonal_adjoint(factor, adjoint):
    product = jnp.dot(
        factor.T, adjoint, precision=lax.Precision.HIGHEST, preferred_element_type=jnp.float32
    )
    lower = jnp.tril(product) - 0.5 * jnp.diag(jnp.diag(product))
    symmetric = lower + lower.T
    half = left_solve(factor, symmetric)
    return 0.5 * left_solve(factor, half.T).T


def bit_reverse(value, bits):
    out = 0
    for k in range(bits):
        out |= ((value >> k) & 1) << (bits - 1 - k)
    return out


def xor_perm(size, mask):
    return [(i, i ^ mask) for i in range(size)]


def make_body(nrow, ncol):
    assert nrow & (nrow - 1) == 0 and ncol & (ncol - 1) == 0
    row_bits = nrow.bit_length() - 1
    ndev = nrow * ncol
    owner_perm = [
        (r * ncol + c, c * nrow + bit_reverse(r, row_bits)) for r in range(nrow) for c in range(ncol)
    ]

    def body(trailing_adjoint, panel, panel_adjoint, diag_factor, diag_adjoint):
        r = lax.axis_index("row")
        c = lax.axis_index("col")

        gathered = panel
        m = 1
        while m < ncol:
            got = lax.ppermute(gathered, "col", xor_perm(ncol, m))
            upper = (c & m) != 0
            gathered = jnp.where(
                upper,
                jnp.concatenate([got, gathered], axis=0),
                jnp.concatenate([gathered, got], axis=0),
            )
            m *= 2

        share = lax.dot_general(
            trailing_adjoint,
            gathered,
            (((0,), (0,)), ((), ())),
            precision=lax.Precision.HIGHEST,
            preferred_element_type=jnp.float32,
        )

        m = 1
        while m < nrow:
            half = share.shape[0] // 2
            low, high = share[:half], share[half:]
            upper = (r & m) != 0
            keep = jnp.where(upper, high, low)
            send = jnp.where(upper, low, high)
            share = keep + lax.ppermute(send, "row", xor_perm(nrow, m))
            m *= 2
        product = lax.ppermute(share, ALL, owner_perm)

        updated = panel_adjoint - 2.0 * product
        off_adjoint = right_solve(diag_factor, updated)
        local_term = jnp.dot(
            off_adjoint.T, panel, precision=lax.Precision.HIGHEST, preferred_element_type=jnp.float32
        )
        rows, cols = diag_adjoint.shape
        placed = lax.dynamic_update_slice(
            jnp.zeros((rows * nrow, cols * ncol), jnp.float32), diag_adjoint, (r * rows, c * cols)
        )
        accumulated = placed - local_term
        m = 1
        while m < ndev:
            accumulated = accumulated + lax.ppermute(accumulated, ALL, xor_perm(ndev, m))
            m *= 2
        return (off_adjoint, diagonal_adjoint(diag_factor, accumulated))

    return body


def solution(mesh):
    return jax.shard_map(
        make_body(mesh.shape["row"], mesh.shape["col"]),
        mesh=mesh,
        in_specs=(
            P("row", "col"),
            P(ALL, None),
            P(ALL, None),
            P(),
            P("row", "col"),
        ),
        out_specs=(P(ALL, None), P()),
        check_vma=False,
    )
```

```python
import jax
import jax.numpy as jnp
from jax import lax
from jax.sharding import PartitionSpec as P

ALL = ("row", "col")


def right_solve(factor, rows):
    return jax.scipy.linalg.solve_triangular(factor, rows.T, lower=True, trans=1).T


def left_solve(factor, matrix):
    return jax.scipy.linalg.solve_triangular(factor, matrix, lower=True, trans=1)


def diagonal_adjoint(factor, adjoint):
    product = jnp.dot(
        factor.T, adjoint, precision=lax.Precision.HIGHEST, preferred_element_type=jnp.float32
    )
    lower = jnp.tril(product) - 0.5 * jnp.diag(jnp.diag(product))
    symmetric = lower + lower.T
    half = left_solve(factor, symmetric)
    return 0.5 * left_solve(factor, half.T).T


def bit_reverse(value, bits):
    out = 0
    for k in range(bits):
        out |= ((value >> k) & 1) << (bits - 1 - k)
    return out


def xor_perm(size, mask):
    return [(i, i ^ mask) for i in range(size)]


def gather_order(ncol):
    bits = [1 << k for k in range(ncol.bit_length() - 1)]
    low = [m for m in bits if m < 8][::-1]
    high = [m for m in bits if m >= 8][::-1]
    return low + high


def all_reduce(value, nrow, ncol):
    ndev = nrow * ncol
    outer = [ncol * m for m in (1, 2) if m < nrow]
    inner = [m for m in (1 << k for k in range(ndev.bit_length() - 1)) if m not in outer]
    for m in outer:
        half = value.shape[0] // 2
        low, high = value[:half], value[half:]
        upper = (lax.axis_index(ALL) & m) != 0
        keep = jnp.where(upper, high, low)
        send = jnp.where(upper, low, high)
        value = keep + lax.ppermute(send, ALL, xor_perm(ndev, m))
    for m in inner:
        value = value + lax.ppermute(value, ALL, xor_perm(ndev, m))
    for m in outer[::-1]:
        got = lax.ppermute(value, ALL, xor_perm(ndev, m))
        upper = (lax.axis_index(ALL) & m) != 0
        value = jnp.where(
            upper, jnp.concatenate([got, value], axis=0), jnp.concatenate([value, got], axis=0)
        )
    return value


def make_body(nrow, ncol):
    assert nrow & (nrow - 1) == 0 and ncol & (ncol - 1) == 0
    row_bits = nrow.bit_length() - 1
    owner_perm = [
        (r * ncol + c, c * nrow + bit_reverse(r, row_bits)) for r in range(nrow) for c in range(ncol)
    ]

    def inner(trailing_adjoint, panel, panel_adjoint, diag_factor, diag_adjoint):
        r = lax.axis_index("row")
        c = lax.axis_index("col")

        gathered = panel
        order = gather_order(ncol)
        for m in order:
            got = lax.ppermute(gathered, "col", xor_perm(ncol, m))
            upper = (c & m) != 0
            gathered = jnp.where(
                upper,
                jnp.concatenate([got, gathered], axis=0),
                jnp.concatenate([gathered, got], axis=0),
            )
        blocks = gathered.reshape((2,) * len(order) + panel.shape)
        nbits = len(order)
        axis_of_bit = {m.bit_length() - 1: nbits - 1 - t for t, m in enumerate(order)}
        perm = [axis_of_bit[nbits - 1 - a] for a in range(nbits)] + [nbits, nbits + 1]
        gathered = blocks.transpose(perm).reshape((ncol * panel.shape[0], panel.shape[1]))

        share = lax.dot_general(
            trailing_adjoint,
            gathered,
            (((0,), (0,)), ((), ())),
            precision=lax.Precision.HIGHEST,
            preferred_element_type=jnp.float32,
        )

        m = 1
        while m < nrow:
            half = share.shape[0] // 2
            low, high = share[:half], share[half:]
            upper = (r & m) != 0
            keep = jnp.where(upper, high, low)
            send = jnp.where(upper, low, high)
            share = keep + lax.ppermute(send, "row", xor_perm(nrow, m))
            m *= 2
        product = lax.ppermute(share, ALL, owner_perm)

        updated = panel_adjoint - 2.0 * product
        off_adjoint = right_solve(diag_factor, updated)
        local_term = jnp.dot(
            off_adjoint.T, panel, precision=lax.Precision.HIGHEST, preferred_element_type=jnp.float32
        )
        rows, cols = diag_adjoint.shape
        placed = lax.dynamic_update_slice(
            jnp.zeros((rows * nrow, cols * ncol), jnp.float32), diag_adjoint, (r * rows, c * cols)
        )
        accumulated = all_reduce(placed - local_term, nrow, ncol)
        return (off_adjoint, diagonal_adjoint(diag_factor, accumulated))

    return inner


def solution(mesh):
    return jax.shard_map(
        make_body(mesh.shape["row"], mesh.shape["col"]),
        mesh=mesh,
        in_specs=(
            P("row", "col"),
            P(ALL, None),
            P(ALL, None),
            P(),
            P("row", "col"),
        ),
        out_specs=(P(ALL, None), P()),
        check_vma=False,
    )
```

```python
import jax
import jax.numpy as jnp
from jax import lax
from jax.sharding import PartitionSpec as P

ALL = ("row", "col")


def right_solve(factor, rows):
    return jax.scipy.linalg.solve_triangular(factor, rows.T, lower=True, trans=1).T


def left_solve(factor, matrix):
    return jax.scipy.linalg.solve_triangular(factor, matrix, lower=True, trans=1)


def diagonal_adjoint(factor, adjoint):
    product = jnp.dot(
        factor.T, adjoint, precision=lax.Precision.HIGHEST, preferred_element_type=jnp.float32
    )
    lower = jnp.tril(product) - 0.5 * jnp.diag(jnp.diag(product))
    symmetric = lower + lower.T
    half = left_solve(factor, symmetric)
    return 0.5 * left_solve(factor, half.T).T


def xor_perm(size, mask):
    return [(i, i ^ mask) for i in range(size)]


def offset(k, masks):
    return sum(m for b, m in enumerate(masks) if (k >> b) & 1)


def position(idx, masks):
    return sum(((idx & m) != 0).astype(jnp.int32) << b for b, m in enumerate(masks))


def exchange(value, axis, size, masks):
    got = [value]
    for k in range(1, 1 << len(masks)):
        got.append(lax.ppermute(value, axis, xor_perm(size, offset(k, masks))))
    return jnp.stack(got)


def gather_step(value, axis, size, masks):
    p = position(lax.axis_index(axis), masks)
    got = exchange(value, axis, size, masks)
    return jnp.concatenate(
        [lax.dynamic_index_in_dim(got, k ^ p, keepdims=False) for k in range(1 << len(masks))], axis=0
    )


def sum_step(value, axis, size, masks):
    p = position(lax.axis_index(axis), masks)
    got = exchange(value, axis, size, masks)
    terms = [lax.dynamic_index_in_dim(got, k ^ p, keepdims=False) for k in range(1 << len(masks))]
    while len(terms) > 1:
        terms = [terms[i] + terms[i + 1] for i in range(0, len(terms), 2)]
    return terms[0]


def scatter_step(value, axis, size, masks):
    n = 1 << len(masks)
    p = position(lax.axis_index(axis), masks)
    chunks = value.reshape((n, value.shape[0] // n) + value.shape[1:])
    total = lax.dynamic_index_in_dim(chunks, p, keepdims=False)
    for k in range(1, n):
        send = lax.dynamic_index_in_dim(chunks, p ^ k, keepdims=False)
        total = total + lax.ppermute(send, axis, xor_perm(size, offset(k, masks)))
    return total


def gather_groups(ncol):
    bits = [1 << k for k in range(ncol.bit_length() - 1)]
    order = [m for m in bits if m < 8][::-1] + [m for m in bits if m >= 8][::-1]
    return [tuple(order[i : i + 2]) for i in range(0, len(order), 2)]


def kept_chunk(idx, groups, nblocks):
    lo, span = 0, nblocks
    for masks in groups:
        n = 1 << len(masks)
        span //= n
        lo += span * sum(((idx & m) != 0) << b for b, m in enumerate(masks))
    return lo


def all_reduce(value, nrow, ncol):
    ndev = nrow * ncol
    bits = [1 << k for k in range(ndev.bit_length() - 1)]
    outer = tuple(ncol * m for m in (1, 2) if m < nrow)
    rest = [m for m in bits if m not in outer]
    inner = [tuple(rest[i : i + 2]) for i in range(0, len(rest), 2)]
    value = scatter_step(value, ALL, ndev, outer)
    for masks in inner:
        value = sum_step(value, ALL, ndev, masks)
    return gather_step(value, ALL, ndev, outer)


def make_body(nrow, ncol):
    assert nrow & (nrow - 1) == 0 and ncol & (ncol - 1) == 0
    row_bits = [1 << k for k in range(nrow.bit_length() - 1)]
    row_groups = [tuple(row_bits[i : i + 2]) for i in range(0, len(row_bits), 2)]
    owner_perm = [
        (r * ncol + c, c * nrow + kept_chunk(r, row_groups, nrow)) for r in range(nrow) for c in range(ncol)
    ]

    def inner(trailing_adjoint, panel, panel_adjoint, diag_factor, diag_adjoint):
        r = lax.axis_index("row")
        c = lax.axis_index("col")

        groups = gather_groups(ncol)
        gathered = panel
        for masks in groups:
            gathered = gather_step(gathered, "col", ncol, masks)
        order = [m for masks in groups for m in masks]
        blocks = gathered.reshape((2,) * len(order) + panel.shape)
        nbits = len(order)
        axis_of_bit = {m.bit_length() - 1: nbits - 1 - t for t, m in enumerate(order)}
        perm = [axis_of_bit[nbits - 1 - a] for a in range(nbits)] + [nbits, nbits + 1]
        gathered = blocks.transpose(perm).reshape((ncol * panel.shape[0], panel.shape[1]))

        share = lax.dot_general(
            trailing_adjoint,
            gathered,
            (((0,), (0,)), ((), ())),
            precision=lax.Precision.HIGHEST,
            preferred_element_type=jnp.float32,
        )

        for masks in row_groups:
            share = scatter_step(share, "row", nrow, masks)
        product = lax.ppermute(share, ALL, owner_perm)

        updated = panel_adjoint - 2.0 * product
        off_adjoint = right_solve(diag_factor, updated)
        local_term = jnp.dot(
            off_adjoint.T, panel, precision=lax.Precision.HIGHEST, preferred_element_type=jnp.float32
        )
        rows, cols = diag_adjoint.shape
        placed = lax.dynamic_update_slice(
            jnp.zeros((rows * nrow, cols * ncol), jnp.float32), diag_adjoint, (r * rows, c * cols)
        )
        accumulated = all_reduce(placed - local_term, nrow, ncol)
        return (off_adjoint, diagonal_adjoint(diag_factor, accumulated))

    return inner


def solution(mesh):
    return jax.shard_map(
        make_body(mesh.shape["row"], mesh.shape["col"]),
        mesh=mesh,
        in_specs=(
            P("row", "col"),
            P(ALL, None),
            P(ALL, None),
            P(),
            P("row", "col"),
        ),
        out_specs=(P(ALL, None), P()),
        check_vma=False,
    )
```

```python
import jax
import jax.numpy as jnp
from jax import lax
from jax.sharding import PartitionSpec as P

ALL = ("row", "col")


def right_solve(factor, rows):
    return jax.scipy.linalg.solve_triangular(factor, rows.T, lower=True, trans=1).T


def left_solve(factor, matrix):
    return jax.scipy.linalg.solve_triangular(factor, matrix, lower=True, trans=1)


def diagonal_adjoint(factor, adjoint):
    product = jnp.dot(
        factor.T, adjoint, precision=lax.Precision.HIGHEST, preferred_element_type=jnp.float32
    )
    lower = jnp.tril(product) - 0.5 * jnp.diag(jnp.diag(product))
    symmetric = lower + lower.T
    half = left_solve(factor, symmetric)
    return 0.5 * left_solve(factor, half.T).T


def xor_perm(size, mask):
    return [(i, i ^ mask) for i in range(size)]


def offset(k, masks):
    return sum(m for b, m in enumerate(masks) if (k >> b) & 1)


def position(idx, masks):
    return sum(((idx & m) != 0).astype(jnp.int32) << b for b, m in enumerate(masks))


def exchange(value, axis, size, masks):
    got = [value]
    for k in range(1, 1 << len(masks)):
        got.append(lax.ppermute(value, axis, xor_perm(size, offset(k, masks))))
    return jnp.stack(got)


def gather_step(value, axis, size, masks):
    p = position(lax.axis_index(axis), masks)
    got = exchange(value, axis, size, masks)
    return jnp.concatenate(
        [lax.dynamic_index_in_dim(got, k ^ p, keepdims=False) for k in range(1 << len(masks))], axis=0
    )


def sum_step(value, axis, size, masks):
    p = position(lax.axis_index(axis), masks)
    got = exchange(value, axis, size, masks)
    terms = [lax.dynamic_index_in_dim(got, k ^ p, keepdims=False) for k in range(1 << len(masks))]
    while len(terms) > 1:
        terms = [terms[i] + terms[i + 1] for i in range(0, len(terms), 2)]
    return terms[0]


def scatter_step(value, axis, size, masks):
    n = 1 << len(masks)
    p = position(lax.axis_index(axis), masks)
    chunks = value.reshape((n, value.shape[0] // n) + value.shape[1:])
    total = lax.dynamic_index_in_dim(chunks, p, keepdims=False)
    for k in range(1, n):
        send = lax.dynamic_index_in_dim(chunks, p ^ k, keepdims=False)
        total = total + lax.ppermute(send, axis, xor_perm(size, offset(k, masks)))
    return total


def gather_groups(ncol):
    bits = [1 << k for k in range(ncol.bit_length() - 1)]
    order = [m for m in bits if m < 8][::-1] + [m for m in bits if m >= 8][::-1]
    return [tuple(order[i : i + 2]) for i in range(0, len(order), 2)]


def kept_chunk(idx, groups, nblocks):
    lo, span = 0, nblocks
    for masks in groups:
        n = 1 << len(masks)
        span //= n
        lo += span * sum(((idx & m) != 0) << b for b, m in enumerate(masks))
    return lo


def all_reduce(value, nrow, ncol):
    ndev = nrow * ncol
    bits = [1 << k for k in range(ndev.bit_length() - 1)]
    outer = tuple(ncol * m for m in (1, 2) if m < nrow)
    rest = [m for m in bits if m not in outer]
    inner = [tuple(rest[i : i + 2]) for i in range(0, len(rest), 2)]
    value = scatter_step(value, ALL, ndev, outer)
    for masks in inner:
        value = sum_step(value, ALL, ndev, masks)
    return gather_step(value, ALL, ndev, outer)


def make_body(nrow, ncol):
    assert nrow & (nrow - 1) == 0 and ncol & (ncol - 1) == 0
    ndev = nrow * ncol
    row_bits = [1 << k for k in range(nrow.bit_length() - 1)]
    row_groups = [tuple(row_bits[i : i + 2]) for i in range(0, len(row_bits), 2)]
    row_groups_natural = row_groups
    col_bits = [1 << k for k in range(ncol.bit_length() - 1)]
    col_groups_natural = [tuple(col_bits[i : i + 2]) for i in range(0, len(col_bits), 2)]
    owner_perm = [
        (r * ncol + c, c * nrow + kept_chunk(r, row_groups, nrow)) for r in range(nrow) for c in range(ncol)
    ]

    def inner(trailing_adjoint, panel, panel_adjoint, diag_factor, diag_adjoint):
        groups = gather_groups(ncol)
        gathered = panel
        for masks in groups:
            gathered = gather_step(gathered, "col", ncol, masks)
        order = [m for masks in groups for m in masks]
        blocks = gathered.reshape((2,) * len(order) + panel.shape)
        nbits = len(order)
        axis_of_bit = {m.bit_length() - 1: nbits - 1 - t for t, m in enumerate(order)}
        perm = [axis_of_bit[nbits - 1 - a] for a in range(nbits)] + [nbits, nbits + 1]
        gathered = blocks.transpose(perm).reshape((ncol * panel.shape[0], panel.shape[1]))

        share = lax.dot_general(
            trailing_adjoint,
            gathered,
            (((0,), (0,)), ((), ())),
            precision=lax.Precision.HIGHEST,
            preferred_element_type=jnp.float32,
        )

        blocks_perm = [(b, (b % nrow) * ncol + b // nrow) for b in range(ndev)]
        col_panel = lax.ppermute(panel, ALL, blocks_perm)
        for masks in row_groups_natural:
            col_panel = gather_step(col_panel, "row", nrow, masks)

        local_term = jnp.dot(
            panel_adjoint.T, panel, precision=lax.Precision.HIGHEST, preferred_element_type=jnp.float32
        ) - 2.0 * jnp.dot(
            share.T, col_panel, precision=lax.Precision.HIGHEST, preferred_element_type=jnp.float32
        )
        total = all_reduce(local_term, nrow, ncol)

        piece = diag_adjoint.T
        for masks in col_groups_natural:
            piece = gather_step(piece, "col", ncol, masks)
        whole = piece.T
        for masks in row_groups_natural:
            whole = gather_step(whole, "row", nrow, masks)

        for masks in row_groups:
            share = scatter_step(share, "row", nrow, masks)
        product = lax.ppermute(share, ALL, owner_perm)
        updated = panel_adjoint - 2.0 * product
        off_adjoint = right_solve(diag_factor, updated)

        accumulated = whole - left_solve(diag_factor, total)
        return (off_adjoint, diagonal_adjoint(diag_factor, accumulated))

    return inner


def solution(mesh):
    return jax.shard_map(
        make_body(mesh.shape["row"], mesh.shape["col"]),
        mesh=mesh,
        in_specs=(
            P("row", "col"),
            P(ALL, None),
            P(ALL, None),
            P(),
            P("row", "col"),
        ),
        out_specs=(P(ALL, None), P()),
        check_vma=False,
    )
```

```python
import jax
import jax.numpy as jnp
from jax import lax
from jax.sharding import PartitionSpec as P

ALL = ("row", "col")


def mm(a, b):
    return jnp.dot(a, b, precision=lax.Precision.HIGHEST, preferred_element_type=jnp.float32)


def lower_inverse(factor, base=32):
    n = factor.shape[0]
    base = min(base, n)
    blocks = jnp.stack([factor[i : i + base, i : i + base] for i in range(0, n, base)])
    eye = jnp.broadcast_to(jnp.eye(base, dtype=factor.dtype), blocks.shape)
    inv = jax.scipy.linalg.solve_triangular(blocks, eye, lower=True)
    s = base
    while s < n:
        first, second = inv[0::2], inv[1::2]
        below = jnp.stack(
            [factor[i + s : i + 2 * s, i : i + s] for i in range(0, n, 2 * s)]
        )
        corner = -jnp.matmul(
            jnp.matmul(second, below, precision=lax.Precision.HIGHEST),
            first,
            precision=lax.Precision.HIGHEST,
        )
        top = jnp.concatenate([first, jnp.zeros_like(first)], axis=2)
        bottom = jnp.concatenate([corner, second], axis=2)
        inv = jnp.concatenate([top, bottom], axis=1)
        s *= 2
    return inv[0]


def diagonal_adjoint(factor, inverse, adjoint):
    product = mm(factor.T, adjoint)
    lower = jnp.tril(product) - 0.5 * jnp.diag(jnp.diag(product))
    symmetric = lower + lower.T
    half = mm(inverse.T, symmetric)
    return 0.5 * mm(half, inverse)


def xor_perm(size, mask):
    return [(i, i ^ mask) for i in range(size)]


def offset(k, masks):
    return sum(m for b, m in enumerate(masks) if (k >> b) & 1)


def position(idx, masks):
    return sum(((idx & m) != 0).astype(jnp.int32) << b for b, m in enumerate(masks))


def exchange(value, axis, size, masks):
    got = [value]
    for k in range(1, 1 << len(masks)):
        got.append(lax.ppermute(value, axis, xor_perm(size, offset(k, masks))))
    return jnp.stack(got)


def gather_step(value, axis, size, masks):
    p = position(lax.axis_index(axis), masks)
    got = exchange(value, axis, size, masks)
    return jnp.concatenate(
        [lax.dynamic_index_in_dim(got, k ^ p, keepdims=False) for k in range(1 << len(masks))], axis=0
    )


def sum_step(value, axis, size, masks):
    p = position(lax.axis_index(axis), masks)
    got = exchange(value, axis, size, masks)
    terms = [lax.dynamic_index_in_dim(got, k ^ p, keepdims=False) for k in range(1 << len(masks))]
    while len(terms) > 1:
        terms = [terms[i] + terms[i + 1] for i in range(0, len(terms), 2)]
    return terms[0]


def scatter_step(value, axis, size, masks):
    n = 1 << len(masks)
    p = position(lax.axis_index(axis), masks)
    chunks = value.reshape((n, value.shape[0] // n) + value.shape[1:])
    total = lax.dynamic_index_in_dim(chunks, p, keepdims=False)
    for k in range(1, n):
        send = lax.dynamic_index_in_dim(chunks, p ^ k, keepdims=False)
        total = total + lax.ppermute(send, axis, xor_perm(size, offset(k, masks)))
    return total


def gather_groups(ncol):
    bits = [1 << k for k in range(ncol.bit_length() - 1)]
    order = [m for m in bits if m < 8][::-1] + [m for m in bits if m >= 8][::-1]
    return [tuple(order[i : i + 2]) for i in range(0, len(order), 2)]


def kept_chunk(idx, groups, nblocks):
    lo, span = 0, nblocks
    for masks in groups:
        n = 1 << len(masks)
        span //= n
        lo += span * sum(((idx & m) != 0) << b for b, m in enumerate(masks))
    return lo


def all_reduce(value, nrow, ncol):
    ndev = nrow * ncol
    bits = [1 << k for k in range(ndev.bit_length() - 1)]
    outer = tuple(ncol * m for m in (1, 2) if m < nrow)
    rest = [m for m in bits if m not in outer]
    inner = [tuple(rest[i : i + 2]) for i in range(0, len(rest), 2)]
    value = scatter_step(value, ALL, ndev, outer)
    for masks in inner:
        value = sum_step(value, ALL, ndev, masks)
    return gather_step(value, ALL, ndev, outer)


def make_body(nrow, ncol):
    assert nrow & (nrow - 1) == 0 and ncol & (ncol - 1) == 0
    ndev = nrow * ncol
    row_bits = [1 << k for k in range(nrow.bit_length() - 1)]
    row_groups = [tuple(row_bits[i : i + 2]) for i in range(0, len(row_bits), 2)]
    row_groups_natural = row_groups
    col_bits = [1 << k for k in range(ncol.bit_length() - 1)]
    col_groups_natural = [tuple(col_bits[i : i + 2]) for i in range(0, len(col_bits), 2)]
    owner_perm = [
        (r * ncol + c, c * nrow + kept_chunk(r, row_groups, nrow)) for r in range(nrow) for c in range(ncol)
    ]

    def inner(trailing_adjoint, panel, panel_adjoint, diag_factor, diag_adjoint):
        inverse = lower_inverse(diag_factor)

        groups = gather_groups(ncol)
        gathered = panel
        for masks in groups:
            gathered = gather_step(gathered, "col", ncol, masks)
        order = [m for masks in groups for m in masks]
        blocks = gathered.reshape((2,) * len(order) + panel.shape)
        nbits = len(order)
        axis_of_bit = {m.bit_length() - 1: nbits - 1 - t for t, m in enumerate(order)}
        perm = [axis_of_bit[nbits - 1 - a] for a in range(nbits)] + [nbits, nbits + 1]
        gathered = blocks.transpose(perm).reshape((ncol * panel.shape[0], panel.shape[1]))

        share = lax.dot_general(
            trailing_adjoint,
            gathered,
            (((0,), (0,)), ((), ())),
            precision=lax.Precision.HIGHEST,
            preferred_element_type=jnp.float32,
        )

        blocks_perm = [(b, (b % nrow) * ncol + b // nrow) for b in range(ndev)]
        col_panel = lax.ppermute(panel, ALL, blocks_perm)
        for masks in row_groups_natural:
            col_panel = gather_step(col_panel, "row", nrow, masks)

        local_term = jnp.dot(
            panel_adjoint.T, panel, precision=lax.Precision.HIGHEST, preferred_element_type=jnp.float32
        ) - 2.0 * jnp.dot(
            share.T, col_panel, precision=lax.Precision.HIGHEST, preferred_element_type=jnp.float32
        )
        total = all_reduce(local_term, nrow, ncol)

        piece = diag_adjoint.T
        for masks in col_groups_natural:
            piece = gather_step(piece, "col", ncol, masks)
        whole = piece.T
        for masks in row_groups_natural:
            whole = gather_step(whole, "row", nrow, masks)

        for masks in row_groups:
            share = scatter_step(share, "row", nrow, masks)
        product = lax.ppermute(share, ALL, owner_perm)
        updated = panel_adjoint - 2.0 * product
        off_adjoint = mm(updated, inverse)

        accumulated = whole - mm(inverse.T, total)
        return (off_adjoint, diagonal_adjoint(diag_factor, inverse, accumulated))

    return inner


def solution(mesh):
    return jax.shard_map(
        make_body(mesh.shape["row"], mesh.shape["col"]),
        mesh=mesh,
        in_specs=(
            P("row", "col"),
            P(ALL, None),
            P(ALL, None),
            P(),
            P("row", "col"),
        ),
        out_specs=(P(ALL, None), P()),
        check_vma=False,
    )
```

```python
import jax
import jax.numpy as jnp
from jax import lax
from jax.sharding import PartitionSpec as P

ALL = ("row", "col")


def mm(a, b):
    return jnp.dot(a, b, precision=lax.Precision.HIGHEST, preferred_element_type=jnp.float32)


def lower_inverse(factor):
    n = factor.shape[0]
    index = jnp.arange(n)
    inverse = jnp.diag(1.0 / jnp.diagonal(factor))
    s = 1
    while s < n:
        inside = (index[:, None] // (2 * s)) == (index[None, :] // (2 * s))
        outside = (index[:, None] // s) != (index[None, :] // s)
        between = jnp.where(inside & outside, factor, 0.0)
        inverse = inverse - mm(mm(inverse, between), inverse)
        s *= 2
    return inverse


def diagonal_adjoint(factor, inverse, adjoint):
    product = mm(factor.T, adjoint)
    lower = jnp.tril(product) - 0.5 * jnp.diag(jnp.diag(product))
    symmetric = lower + lower.T
    half = mm(inverse.T, symmetric)
    return 0.5 * mm(half, inverse)


def xor_perm(size, mask):
    return [(i, i ^ mask) for i in range(size)]


def offset(k, masks):
    return sum(m for b, m in enumerate(masks) if (k >> b) & 1)


def position(idx, masks):
    return sum(((idx & m) != 0).astype(jnp.int32) << b for b, m in enumerate(masks))


def exchange(value, axis, size, masks):
    got = [value]
    for k in range(1, 1 << len(masks)):
        got.append(lax.ppermute(value, axis, xor_perm(size, offset(k, masks))))
    return jnp.stack(got)


def gather_step(value, axis, size, masks):
    p = position(lax.axis_index(axis), masks)
    got = exchange(value, axis, size, masks)
    return jnp.concatenate(
        [lax.dynamic_index_in_dim(got, k ^ p, keepdims=False) for k in range(1 << len(masks))], axis=0
    )


def sum_step(value, axis, size, masks):
    p = position(lax.axis_index(axis), masks)
    got = exchange(value, axis, size, masks)
    terms = [lax.dynamic_index_in_dim(got, k ^ p, keepdims=False) for k in range(1 << len(masks))]
    while len(terms) > 1:
        terms = [terms[i] + terms[i + 1] for i in range(0, len(terms), 2)]
    return terms[0]


def scatter_step(value, axis, size, masks):
    n = 1 << len(masks)
    p = position(lax.axis_index(axis), masks)
    chunks = value.reshape((n, value.shape[0] // n) + value.shape[1:])
    total = lax.dynamic_index_in_dim(chunks, p, keepdims=False)
    for k in range(1, n):
        send = lax.dynamic_index_in_dim(chunks, p ^ k, keepdims=False)
        total = total + lax.ppermute(send, axis, xor_perm(size, offset(k, masks)))
    return total


def gather_groups(ncol):
    bits = [1 << k for k in range(ncol.bit_length() - 1)]
    order = [m for m in bits if m < 8][::-1] + [m for m in bits if m >= 8][::-1]
    return [tuple(order[i : i + 2]) for i in range(0, len(order), 2)]


def kept_chunk(idx, groups, nblocks):
    lo, span = 0, nblocks
    for masks in groups:
        n = 1 << len(masks)
        span //= n
        lo += span * sum(((idx & m) != 0) << b for b, m in enumerate(masks))
    return lo


def all_reduce(value, nrow, ncol):
    ndev = nrow * ncol
    bits = [1 << k for k in range(ndev.bit_length() - 1)]
    outer = tuple(ncol * m for m in (1, 2) if m < nrow)
    rest = [m for m in bits if m not in outer]
    inner = [tuple(rest[i : i + 2]) for i in range(0, len(rest), 2)]
    value = scatter_step(value, ALL, ndev, outer)
    for masks in inner:
        value = sum_step(value, ALL, ndev, masks)
    return gather_step(value, ALL, ndev, outer)


def make_body(nrow, ncol):
    assert nrow & (nrow - 1) == 0 and ncol & (ncol - 1) == 0
    row_bits = [1 << k for k in range(nrow.bit_length() - 1)]
    row_groups = [tuple(row_bits[i : i + 2]) for i in range(0, len(row_bits), 2)]
    owner_perm = [
        (r * ncol + c, c * nrow + kept_chunk(r, row_groups, nrow)) for r in range(nrow) for c in range(ncol)
    ]

    def inner(trailing_adjoint, panel, panel_adjoint, diag_factor, diag_adjoint):
        r = lax.axis_index("row")
        c = lax.axis_index("col")
        inverse = lower_inverse(diag_factor)

        groups = gather_groups(ncol)
        gathered = panel
        for masks in groups:
            gathered = gather_step(gathered, "col", ncol, masks)
        order = [m for masks in groups for m in masks]
        blocks = gathered.reshape((2,) * len(order) + panel.shape)
        nbits = len(order)
        axis_of_bit = {m.bit_length() - 1: nbits - 1 - t for t, m in enumerate(order)}
        perm = [axis_of_bit[nbits - 1 - a] for a in range(nbits)] + [nbits, nbits + 1]
        gathered = blocks.transpose(perm).reshape((ncol * panel.shape[0], panel.shape[1]))

        share = lax.dot_general(
            trailing_adjoint,
            gathered,
            (((0,), (0,)), ((), ())),
            precision=lax.Precision.HIGHEST,
            preferred_element_type=jnp.float32,
        )

        for masks in row_groups:
            share = scatter_step(share, "row", nrow, masks)
        product = lax.ppermute(share, ALL, owner_perm)

        updated = panel_adjoint - 2.0 * product
        off_adjoint = mm(updated, inverse)
        local_term = jnp.dot(
            off_adjoint.T, panel, precision=lax.Precision.HIGHEST, preferred_element_type=jnp.float32
        )
        rows, cols = diag_adjoint.shape
        placed = lax.dynamic_update_slice(
            jnp.zeros((rows * nrow, cols * ncol), jnp.float32), diag_adjoint, (r * rows, c * cols)
        )
        accumulated = all_reduce(placed - local_term, nrow, ncol)
        return (off_adjoint, diagonal_adjoint(diag_factor, inverse, accumulated))

    return inner


def solution(mesh):
    return jax.shard_map(
        make_body(mesh.shape["row"], mesh.shape["col"]),
        mesh=mesh,
        in_specs=(
            P("row", "col"),
            P(ALL, None),
            P(ALL, None),
            P(),
            P("row", "col"),
        ),
        out_specs=(P(ALL, None), P()),
        check_vma=False,
    )
```

```python
import jax
import jax.numpy as jnp
from jax import lax
from jax.sharding import PartitionSpec as P

ALL = ("row", "col")


def mm(a, b):
    return jnp.dot(a, b, precision=lax.Precision.HIGHEST, preferred_element_type=jnp.float32)


def lower_inverse(factor):
    n = factor.shape[0]
    index = jnp.arange(n)
    inverse = jnp.diag(1.0 / jnp.diagonal(factor))
    s = 1
    while s < n:
        inside = (index[:, None] // (2 * s)) == (index[None, :] // (2 * s))
        outside = (index[:, None] // s) != (index[None, :] // s)
        between = jnp.where(inside & outside, factor, 0.0)
        inverse = inverse - mm(mm(inverse, between), inverse)
        s *= 2
    return inverse


def diagonal_adjoint(factor, inverse, adjoint):
    product = mm(factor.T, adjoint)
    lower = jnp.tril(product) - 0.5 * jnp.diag(jnp.diag(product))
    symmetric = lower + lower.T
    half = mm(inverse.T, symmetric)
    return 0.5 * mm(half, inverse)


def xor_perm(size, mask):
    return [(i, i ^ mask) for i in range(size)]


def offset(k, masks):
    return sum(m for b, m in enumerate(masks) if (k >> b) & 1)


def position(idx, masks):
    return sum(((idx & m) != 0).astype(jnp.int32) << b for b, m in enumerate(masks))


def exchange(value, axis, size, masks):
    got = [value]
    for k in range(1, 1 << len(masks)):
        got.append(lax.ppermute(value, axis, xor_perm(size, offset(k, masks))))
    return jnp.stack(got)


def gather_step(value, axis, size, masks):
    p = position(lax.axis_index(axis), masks)
    got = exchange(value, axis, size, masks)
    return jnp.concatenate(
        [lax.dynamic_index_in_dim(got, k ^ p, keepdims=False) for k in range(1 << len(masks))], axis=0
    )


def sum_step(value, axis, size, masks):
    p = position(lax.axis_index(axis), masks)
    got = exchange(value, axis, size, masks)
    terms = [lax.dynamic_index_in_dim(got, k ^ p, keepdims=False) for k in range(1 << len(masks))]
    while len(terms) > 1:
        terms = [terms[i] + terms[i + 1] for i in range(0, len(terms), 2)]
    return terms[0]


def scatter_step(value, axis, size, masks):
    n = 1 << len(masks)
    p = position(lax.axis_index(axis), masks)
    chunks = value.reshape((n, value.shape[0] // n) + value.shape[1:])
    total = lax.dynamic_index_in_dim(chunks, p, keepdims=False)
    for k in range(1, n):
        send = lax.dynamic_index_in_dim(chunks, p ^ k, keepdims=False)
        total = total + lax.ppermute(send, axis, xor_perm(size, offset(k, masks)))
    return total


def gather_groups(ncol):
    bits = [1 << k for k in range(ncol.bit_length() - 1)]
    low = [m for m in bits if m < 8][::-1]
    high = [m for m in bits if m >= 8]
    groups = [tuple(low[i : i + 2]) for i in range(0, len(low), 2)]
    return groups + [tuple(high[i : i + 2]) for i in range(0, len(high), 2)]


def kept_chunk(idx, groups, nblocks):
    lo, span = 0, nblocks
    for masks in groups:
        n = 1 << len(masks)
        span //= n
        lo += span * sum(((idx & m) != 0) << b for b, m in enumerate(masks))
    return lo


def all_reduce(value, nrow, ncol):
    ndev = nrow * ncol
    bits = [1 << k for k in range(ndev.bit_length() - 1)]
    outer = tuple(ncol * m for m in (1, 2) if m < nrow)
    rest = [m for m in bits if m not in outer]
    inner = [tuple(rest[i : i + 2]) for i in range(0, len(rest), 2)]
    value = scatter_step(value, ALL, ndev, outer)
    for masks in inner:
        value = sum_step(value, ALL, ndev, masks)
    return gather_step(value, ALL, ndev, outer)


def make_body(nrow, ncol):
    assert nrow & (nrow - 1) == 0 and ncol & (ncol - 1) == 0
    ndev = nrow * ncol
    row_bits = [1 << k for k in range(nrow.bit_length() - 1)]
    row_groups = [tuple(row_bits[i : i + 2]) for i in range(0, len(row_bits), 2)]
    blocks_perm = [(b, (b % nrow) * ncol + b // nrow) for b in range(ndev)]
    owner_perm = [
        (r * ncol + c, c * nrow + kept_chunk(r, row_groups, nrow)) for r in range(nrow) for c in range(ncol)
    ]

    def inner(trailing_adjoint, panel, panel_adjoint, diag_factor, diag_adjoint):
        r = lax.axis_index("row")
        c = lax.axis_index("col")
        inverse = lower_inverse(diag_factor)

        groups = gather_groups(ncol)
        gathered = panel
        for masks in groups:
            gathered = gather_step(gathered, "col", ncol, masks)
        order = [m for masks in groups for m in masks]
        blocks = gathered.reshape((2,) * len(order) + panel.shape)
        nbits = len(order)
        axis_of_bit = {m.bit_length() - 1: nbits - 1 - t for t, m in enumerate(order)}
        perm = [axis_of_bit[nbits - 1 - a] for a in range(nbits)] + [nbits, nbits + 1]
        gathered = blocks.transpose(perm).reshape((ncol * panel.shape[0], panel.shape[1]))

        share = lax.dot_general(
            trailing_adjoint,
            gathered,
            (((0,), (0,)), ((), ())),
            precision=lax.Precision.HIGHEST,
            preferred_element_type=jnp.float32,
        )

        col_panel = lax.ppermute(panel, ALL, blocks_perm)
        for masks in row_groups:
            col_panel = gather_step(col_panel, "row", nrow, masks)

        local_term = mm(panel_adjoint.T, panel) - 2.0 * mm(share.T, col_panel)
        rows, cols = diag_adjoint.shape
        placed = lax.dynamic_update_slice(
            jnp.zeros((rows * nrow, cols * ncol), jnp.float32), diag_adjoint, (r * rows, c * cols)
        )
        summed = all_reduce(jnp.concatenate([local_term, placed], axis=0), nrow, ncol)
        total, whole = summed[: local_term.shape[0]], summed[local_term.shape[0] :]

        for masks in row_groups:
            share = scatter_step(share, "row", nrow, masks)
        product = lax.ppermute(share, ALL, owner_perm)
        updated = panel_adjoint - 2.0 * product
        off_adjoint = mm(updated, inverse)

        accumulated = whole - mm(inverse.T, total)
        return (off_adjoint, diagonal_adjoint(diag_factor, inverse, accumulated))

    return inner


def solution(mesh):
    return jax.shard_map(
        make_body(mesh.shape["row"], mesh.shape["col"]),
        mesh=mesh,
        in_specs=(
            P("row", "col"),
            P(ALL, None),
            P(ALL, None),
            P(),
            P("row", "col"),
        ),
        out_specs=(P(ALL, None), P()),
        check_vma=False,
    )
```

```python
import jax
import jax.numpy as jnp
from jax import lax
from jax.sharding import PartitionSpec as P

ALL = ("row", "col")


def mm(a, b):
    return jnp.dot(a, b, precision=lax.Precision.HIGHEST, preferred_element_type=jnp.float32)


def lower_inverse(factor):
    n = factor.shape[0]
    index = jnp.arange(n)
    inverse = jnp.diag(1.0 / jnp.diagonal(factor))
    s = 1
    while s < n:
        inside = (index[:, None] // (2 * s)) == (index[None, :] // (2 * s))
        outside = (index[:, None] // s) != (index[None, :] // s)
        between = jnp.where(inside & outside, factor, 0.0)
        inverse = inverse - mm(mm(inverse, between), inverse)
        s *= 2
    return inverse


def diagonal_adjoint(factor, inverse, adjoint):
    product = mm(factor.T, adjoint)
    lower = jnp.tril(product) - 0.5 * jnp.diag(jnp.diag(product))
    symmetric = lower + lower.T
    half = mm(inverse.T, symmetric)
    return 0.5 * mm(half, inverse)


def xor_perm(size, mask):
    return [(i, i ^ mask) for i in range(size)]


def offset(k, masks):
    return sum(m for b, m in enumerate(masks) if (k >> b) & 1)


def position(idx, masks):
    return sum(((idx & m) != 0).astype(jnp.int32) << b for b, m in enumerate(masks))


def exchange(value, axis, size, masks):
    got = [value]
    for k in range(1, 1 << len(masks)):
        got.append(lax.ppermute(value, axis, xor_perm(size, offset(k, masks))))
    return jnp.stack(got)


def gather_step(value, axis, size, masks):
    p = position(lax.axis_index(axis), masks)
    got = exchange(value, axis, size, masks)
    return jnp.concatenate(
        [lax.dynamic_index_in_dim(got, k ^ p, keepdims=False) for k in range(1 << len(masks))], axis=0
    )


def sum_step(value, axis, size, masks):
    p = position(lax.axis_index(axis), masks)
    got = exchange(value, axis, size, masks)
    terms = [lax.dynamic_index_in_dim(got, k ^ p, keepdims=False) for k in range(1 << len(masks))]
    while len(terms) > 1:
        terms = [terms[i] + terms[i + 1] for i in range(0, len(terms), 2)]
    return terms[0]


def scatter_step(value, axis, size, masks):
    n = 1 << len(masks)
    p = position(lax.axis_index(axis), masks)
    chunks = value.reshape((n, value.shape[0] // n) + value.shape[1:])
    total = lax.dynamic_index_in_dim(chunks, p, keepdims=False)
    for k in range(1, n):
        send = lax.dynamic_index_in_dim(chunks, p ^ k, keepdims=False)
        total = total + lax.ppermute(send, axis, xor_perm(size, offset(k, masks)))
    return total


def gather_groups(ncol):
    bits = [1 << k for k in range(ncol.bit_length() - 1)]
    low = [m for m in bits if m < 8][::-1]
    high = [m for m in bits if m >= 8]
    groups = [tuple(high[i : i + 2]) for i in range(0, len(high), 2)]
    return groups + [tuple(low[i : i + 2]) for i in range(0, len(low), 2)]


def kept_chunk(idx, groups, nblocks):
    lo, span = 0, nblocks
    for masks in groups:
        n = 1 << len(masks)
        span //= n
        lo += span * sum(((idx & m) != 0) << b for b, m in enumerate(masks))
    return lo


def all_reduce(value, nrow, ncol):
    ndev = nrow * ncol
    bits = [1 << k for k in range(ndev.bit_length() - 1)]
    outer = tuple(ncol * m for m in (1, 2) if m < nrow)
    rest = [m for m in bits if m not in outer]
    inner = [tuple(rest[i : i + 2]) for i in range(0, len(rest), 2)]
    value = scatter_step(value, ALL, ndev, outer)
    for masks in inner:
        value = sum_step(value, ALL, ndev, masks)
    return gather_step(value, ALL, ndev, outer)


def make_body(nrow, ncol):
    assert nrow & (nrow - 1) == 0 and ncol & (ncol - 1) == 0
    row_bits = [1 << k for k in range(nrow.bit_length() - 1)]
    row_groups = [tuple(row_bits[i : i + 2]) for i in range(0, len(row_bits), 2)]
    owner_perm = [
        (r * ncol + c, c * nrow + kept_chunk(r, row_groups, nrow)) for r in range(nrow) for c in range(ncol)
    ]

    def inner(trailing_adjoint, panel, panel_adjoint, diag_factor, diag_adjoint):
        r = lax.axis_index("row")
        c = lax.axis_index("col")
        inverse = lower_inverse(diag_factor)

        groups = gather_groups(ncol)
        gathered = panel
        for masks in groups:
            gathered = gather_step(gathered, "col", ncol, masks)
        order = [m for masks in groups for m in masks]
        blocks = gathered.reshape((2,) * len(order) + panel.shape)
        nbits = len(order)
        axis_of_bit = {m.bit_length() - 1: nbits - 1 - t for t, m in enumerate(order)}
        perm = [axis_of_bit[nbits - 1 - a] for a in range(nbits)] + [nbits, nbits + 1]
        gathered = blocks.transpose(perm).reshape((ncol * panel.shape[0], panel.shape[1]))

        share = lax.dot_general(
            trailing_adjoint,
            gathered,
            (((0,), (0,)), ((), ())),
            precision=lax.Precision.HIGHEST,
            preferred_element_type=jnp.float32,
        )

        for masks in row_groups:
            share = scatter_step(share, "row", nrow, masks)
        product = lax.ppermute(share, ALL, owner_perm)

        updated = panel_adjoint - 2.0 * product
        off_adjoint = mm(updated, inverse)
        local_term = jnp.dot(
            off_adjoint.T, panel, precision=lax.Precision.HIGHEST, preferred_element_type=jnp.float32
        )
        rows, cols = diag_adjoint.shape
        placed = lax.dynamic_update_slice(
            jnp.zeros((rows * nrow, cols * ncol), jnp.float32), diag_adjoint, (r * rows, c * cols)
        )
        accumulated = all_reduce(placed - local_term, nrow, ncol)
        return (off_adjoint, diagonal_adjoint(diag_factor, inverse, accumulated))

    return inner


def solution(mesh):
    return jax.shard_map(
        make_body(mesh.shape["row"], mesh.shape["col"]),
        mesh=mesh,
        in_specs=(
            P("row", "col"),
            P(ALL, None),
            P(ALL, None),
            P(),
            P("row", "col"),
        ),
        out_specs=(P(ALL, None), P()),
        check_vma=False,
    )
```

```python
import jax
import jax.numpy as jnp
from jax import lax
from jax.sharding import PartitionSpec as P

ALL = ("row", "col")


def mm(a, b):
    return jnp.dot(a, b, precision=lax.Precision.HIGHEST, preferred_element_type=jnp.float32)


def lower_inverse(factor):
    n = factor.shape[0]
    index = jnp.arange(n)
    inverse = jnp.diag(1.0 / jnp.diagonal(factor))
    s = 1
    while s < n:
        inside = (index[:, None] // (2 * s)) == (index[None, :] // (2 * s))
        outside = (index[:, None] // s) != (index[None, :] // s)
        between = jnp.where(inside & outside, factor, 0.0)
        inverse = inverse - mm(mm(inverse, between), inverse)
        s *= 2
    return inverse


def diagonal_adjoint(factor, inverse, adjoint):
    product = mm(factor.T, adjoint)
    lower = jnp.tril(product) - 0.5 * jnp.diag(jnp.diag(product))
    symmetric = lower + lower.T
    half = mm(inverse.T, symmetric)
    return 0.5 * mm(half, inverse)


def xor_perm(size, mask):
    return [(i, i ^ mask) for i in range(size)]


def offset(k, masks):
    return sum(m for b, m in enumerate(masks) if (k >> b) & 1)


def position(idx, masks):
    return sum(((idx & m) != 0).astype(jnp.int32) << b for b, m in enumerate(masks))


def exchange(value, axis, size, masks):
    got = [value]
    for k in range(1, 1 << len(masks)):
        got.append(lax.ppermute(value, axis, xor_perm(size, offset(k, masks))))
    return jnp.stack(got)


def gather_step(value, axis, size, masks):
    p = position(lax.axis_index(axis), masks)
    got = exchange(value, axis, size, masks)
    return jnp.concatenate(
        [lax.dynamic_index_in_dim(got, k ^ p, keepdims=False) for k in range(1 << len(masks))], axis=0
    )


def sum_step(value, axis, size, masks):
    p = position(lax.axis_index(axis), masks)
    got = exchange(value, axis, size, masks)
    terms = [lax.dynamic_index_in_dim(got, k ^ p, keepdims=False) for k in range(1 << len(masks))]
    while len(terms) > 1:
        terms = [terms[i] + terms[i + 1] for i in range(0, len(terms), 2)]
    return terms[0]


def scatter_step(value, axis, size, masks):
    n = 1 << len(masks)
    p = position(lax.axis_index(axis), masks)
    chunks = value.reshape((n, value.shape[0] // n) + value.shape[1:])
    total = lax.dynamic_index_in_dim(chunks, p, keepdims=False)
    for k in range(1, n):
        send = lax.dynamic_index_in_dim(chunks, p ^ k, keepdims=False)
        total = total + lax.ppermute(send, axis, xor_perm(size, offset(k, masks)))
    return total


def gather_groups(ncol):
    bits = [1 << k for k in range(ncol.bit_length() - 1)]
    low = [m for m in bits if m < 8][::-1]
    high = [m for m in bits if m >= 8]
    groups = [tuple(low[i : i + 2]) for i in range(0, len(low), 2)]
    return groups + [tuple(high[i : i + 2]) for i in range(0, len(high), 2)]


def kept_chunk(idx, groups, nblocks):
    lo, span = 0, nblocks
    for masks in groups:
        n = 1 << len(masks)
        span //= n
        lo += span * sum(((idx & m) != 0) << b for b, m in enumerate(masks))
    return lo


def all_reduce(value, nrow, ncol):
    ndev = nrow * ncol
    bits = [1 << k for k in range(ndev.bit_length() - 1)]
    outer = tuple(ncol * m for m in (1, 2) if m < nrow)
    rest = [m for m in bits if m not in outer]
    inner = [tuple(rest[i : i + 2]) for i in range(0, len(rest), 2)]
    value = scatter_step(value, ALL, ndev, outer)
    for masks in inner:
        value = sum_step(value, ALL, ndev, masks)
    return gather_step(value, ALL, ndev, outer)


def make_body(nrow, ncol):
    assert nrow & (nrow - 1) == 0 and ncol & (ncol - 1) == 0
    row_bits = [1 << k for k in range(nrow.bit_length() - 1)]
    row_groups = [tuple(row_bits[i : i + 2]) for i in range(0, len(row_bits), 2)]
    owner_perm = [
        (r * ncol + c, c * nrow + kept_chunk(r, row_groups, nrow)) for r in range(nrow) for c in range(ncol)
    ]

    fetch_perm = [(dst, src) for src, dst in owner_perm]

    def inner(trailing_adjoint, panel, panel_adjoint, diag_factor, diag_adjoint):
        r = lax.axis_index("row")
        c = lax.axis_index("col")
        inverse = lower_inverse(diag_factor)
        own_rows = lax.ppermute(jnp.stack([panel, panel_adjoint]), ALL, fetch_perm)

        groups = gather_groups(ncol)
        gathered = panel
        for masks in groups:
            gathered = gather_step(gathered, "col", ncol, masks)
        order = [m for masks in groups for m in masks]
        blocks = gathered.reshape((2,) * len(order) + panel.shape)
        nbits = len(order)
        axis_of_bit = {m.bit_length() - 1: nbits - 1 - t for t, m in enumerate(order)}
        perm = [axis_of_bit[nbits - 1 - a] for a in range(nbits)] + [nbits, nbits + 1]
        gathered = blocks.transpose(perm).reshape((ncol * panel.shape[0], panel.shape[1]))

        share = lax.dot_general(
            trailing_adjoint,
            gathered,
            (((0,), (0,)), ((), ())),
            precision=lax.Precision.HIGHEST,
            preferred_element_type=jnp.float32,
        )

        for masks in row_groups:
            share = scatter_step(share, "row", nrow, masks)
        updated = own_rows[1] - 2.0 * share
        off_rows = mm(updated, inverse)
        local_term = mm(off_rows.T, own_rows[0])
        off_adjoint = lax.ppermute(off_rows, ALL, owner_perm)
        rows, cols = diag_adjoint.shape
        placed = lax.dynamic_update_slice(
            jnp.zeros((rows * nrow, cols * ncol), jnp.float32), diag_adjoint, (r * rows, c * cols)
        )
        accumulated = all_reduce(placed - local_term, nrow, ncol)
        return (off_adjoint, diagonal_adjoint(diag_factor, inverse, accumulated))

    return inner


def solution(mesh):
    return jax.shard_map(
        make_body(mesh.shape["row"], mesh.shape["col"]),
        mesh=mesh,
        in_specs=(
            P("row", "col"),
            P(ALL, None),
            P(ALL, None),
            P(),
            P("row", "col"),
        ),
        out_specs=(P(ALL, None), P()),
        check_vma=False,
    )
```

```python
import jax
import jax.numpy as jnp
from jax import lax
from jax.sharding import PartitionSpec as P

ALL = ("row", "col")


def mm(a, b):
    return jnp.dot(a, b, precision=lax.Precision.HIGHEST, preferred_element_type=jnp.float32)


def lower_inverse(factor):
    n = factor.shape[0]
    index = jnp.arange(n)
    inverse = jnp.diag(1.0 / jnp.diagonal(factor))
    s = 1
    while s < n:
        inside = (index[:, None] // (2 * s)) == (index[None, :] // (2 * s))
        outside = (index[:, None] // s) != (index[None, :] // s)
        between = jnp.where(inside & outside, factor, 0.0)
        inverse = inverse - mm(mm(inverse, between), inverse)
        s *= 2
    return inverse


def diagonal_adjoint(factor, inverse, adjoint):
    product = mm(factor.T, adjoint)
    lower = jnp.tril(product) - 0.5 * jnp.diag(jnp.diag(product))
    symmetric = lower + lower.T
    half = mm(inverse.T, symmetric)
    return 0.5 * mm(half, inverse)


def xor_perm(size, mask):
    return [(i, i ^ mask) for i in range(size)]


def offset(k, masks):
    return sum(m for b, m in enumerate(masks) if (k >> b) & 1)


def position(idx, masks):
    return sum(((idx & m) != 0).astype(jnp.int32) << b for b, m in enumerate(masks))


def exchange(value, axis, size, masks):
    got = [value]
    for k in range(1, 1 << len(masks)):
        got.append(lax.ppermute(value, axis, xor_perm(size, offset(k, masks))))
    return jnp.stack(got)


def gather_step(value, axis, size, masks):
    p = position(lax.axis_index(axis), masks)
    got = exchange(value, axis, size, masks)
    return jnp.concatenate(
        [lax.dynamic_index_in_dim(got, k ^ p, keepdims=False) for k in range(1 << len(masks))], axis=0
    )


def sum_step(value, axis, size, masks):
    p = position(lax.axis_index(axis), masks)
    got = exchange(value, axis, size, masks)
    terms = [lax.dynamic_index_in_dim(got, k ^ p, keepdims=False) for k in range(1 << len(masks))]
    while len(terms) > 1:
        terms = [terms[i] + terms[i + 1] for i in range(0, len(terms), 2)]
    return terms[0]


def scatter_step(value, axis, size, masks):
    n = 1 << len(masks)
    p = position(lax.axis_index(axis), masks)
    chunks = value.reshape((n, value.shape[0] // n) + value.shape[1:])
    total = lax.dynamic_index_in_dim(chunks, p, keepdims=False)
    for k in range(1, n):
        send = lax.dynamic_index_in_dim(chunks, p ^ k, keepdims=False)
        total = total + lax.ppermute(send, axis, xor_perm(size, offset(k, masks)))
    return total


def gather_groups(ncol):
    bits = [1 << k for k in range(ncol.bit_length() - 1)]
    low = [m for m in bits if m < 8][::-1]
    high = [m for m in bits if m >= 8]
    groups = [tuple(low[i : i + 2]) for i in range(0, len(low), 2)]
    return groups + [tuple(high[i : i + 2]) for i in range(0, len(high), 2)]


def kept_chunk(idx, groups, nblocks):
    lo, span = 0, nblocks
    for masks in groups:
        n = 1 << len(masks)
        span //= n
        lo += span * sum(((idx & m) != 0) << b for b, m in enumerate(masks))
    return lo


def all_reduce(value, nrow, ncol):
    ndev = nrow * ncol
    bits = [1 << k for k in range(ndev.bit_length() - 1)]
    outer = tuple(ncol * m for m in (1, 2) if m < nrow)
    rest = [m for m in bits if m not in outer]
    inner = [tuple(rest[i : i + 2]) for i in range(0, len(rest), 2)]
    value = scatter_step(value, ALL, ndev, outer)
    for masks in inner:
        value = sum_step(value, ALL, ndev, masks)
    return gather_step(value, ALL, ndev, outer)


def make_body(nrow, ncol):
    assert nrow & (nrow - 1) == 0 and ncol & (ncol - 1) == 0
    row_bits = [1 << k for k in range(nrow.bit_length() - 1)]
    row_groups = [tuple(row_bits[i : i + 2]) for i in range(0, len(row_bits), 2)]
    owner_perm = [
        (r * ncol + c, c * nrow + kept_chunk(r, row_groups, nrow)) for r in range(nrow) for c in range(ncol)
    ]

    q = ncol // nrow
    col_block_perm = [
        (big * ncol + small, (small // q) * ncol + q * big + small % q)
        for big in range(nrow)
        for small in range(ncol)
    ]

    def inner(trailing_adjoint, panel, panel_adjoint, diag_factor, diag_adjoint):
        r = lax.axis_index("row")
        c = lax.axis_index("col")
        inverse = lower_inverse(diag_factor)

        groups = gather_groups(ncol)
        gathered = panel
        for masks in groups:
            gathered = gather_step(gathered, "col", ncol, masks)
        order = [m for masks in groups for m in masks]
        blocks = gathered.reshape((2,) * len(order) + panel.shape)
        nbits = len(order)
        axis_of_bit = {m.bit_length() - 1: nbits - 1 - t for t, m in enumerate(order)}
        perm = [axis_of_bit[nbits - 1 - a] for a in range(nbits)] + [nbits, nbits + 1]
        gathered = blocks.transpose(perm).reshape((ncol * panel.shape[0], panel.shape[1]))

        share = lax.dot_general(
            trailing_adjoint,
            gathered,
            (((0,), (0,)), ((), ())),
            precision=lax.Precision.HIGHEST,
            preferred_element_type=jnp.float32,
        )

        span = share.shape[0]
        pick = lax.dynamic_slice_in_dim(gathered, (c % q) * span, span, 0)
        col_panel = lax.ppermute(pick, ALL, col_block_perm)

        local_term = mm(inverse.T, mm(panel_adjoint.T, panel) - 2.0 * mm(share.T, col_panel))
        rows, cols = diag_adjoint.shape
        placed = lax.dynamic_update_slice(
            jnp.zeros((rows * nrow, cols * ncol), jnp.float32), diag_adjoint, (r * rows, c * cols)
        )
        accumulated = all_reduce(placed - local_term, nrow, ncol)

        for masks in row_groups:
            share = scatter_step(share, "row", nrow, masks)
        product = lax.ppermute(share, ALL, owner_perm)
        updated = panel_adjoint - 2.0 * product
        off_adjoint = mm(updated, inverse)
        return (off_adjoint, diagonal_adjoint(diag_factor, inverse, accumulated))

    return inner


def solution(mesh):
    return jax.shard_map(
        make_body(mesh.shape["row"], mesh.shape["col"]),
        mesh=mesh,
        in_specs=(
            P("row", "col"),
            P(ALL, None),
            P(ALL, None),
            P(),
            P("row", "col"),
        ),
        out_specs=(P(ALL, None), P()),
        check_vma=False,
    )
```

```python
import jax
import jax.numpy as jnp
from jax import lax
from jax.sharding import PartitionSpec as P

ALL = ("row", "col")


def mm(a, b):
    return jnp.dot(a, b, precision=lax.Precision.HIGHEST, preferred_element_type=jnp.float32)


def lower_inverse(factor):
    n = factor.shape[0]
    index = jnp.arange(n)
    inverse = jnp.diag(1.0 / jnp.diagonal(factor))
    s = 1
    while s < n:
        inside = (index[:, None] // (2 * s)) == (index[None, :] // (2 * s))
        outside = (index[:, None] // s) != (index[None, :] // s)
        between = jnp.where(inside & outside, factor, 0.0)
        inverse = inverse - mm(mm(inverse, between), inverse)
        s *= 2
    return inverse


def diagonal_adjoint(factor, inverse, adjoint):
    product = mm(factor.T, adjoint)
    lower = jnp.tril(product) - 0.5 * jnp.diag(jnp.diag(product))
    symmetric = lower + lower.T
    half = mm(inverse.T, symmetric)
    return 0.5 * mm(half, inverse)


def xor_perm(size, mask):
    return [(i, i ^ mask) for i in range(size)]


def offset(k, masks):
    return sum(m for b, m in enumerate(masks) if (k >> b) & 1)


def position(idx, masks):
    return sum(((idx & m) != 0).astype(jnp.int32) << b for b, m in enumerate(masks))


def exchange(value, axis, size, masks):
    got = [value]
    for k in range(1, 1 << len(masks)):
        got.append(lax.ppermute(value, axis, xor_perm(size, offset(k, masks))))
    return jnp.stack(got)


def gather_step(value, axis, size, masks):
    p = position(lax.axis_index(axis), masks)
    got = exchange(value, axis, size, masks)
    return jnp.concatenate(
        [lax.dynamic_index_in_dim(got, k ^ p, keepdims=False) for k in range(1 << len(masks))], axis=0
    )


def sum_step(value, axis, size, masks):
    p = position(lax.axis_index(axis), masks)
    got = exchange(value, axis, size, masks)
    terms = [lax.dynamic_index_in_dim(got, k ^ p, keepdims=False) for k in range(1 << len(masks))]
    while len(terms) > 1:
        terms = [terms[i] + terms[i + 1] for i in range(0, len(terms), 2)]
    return terms[0]


def scatter_step(value, axis, size, masks):
    n = 1 << len(masks)
    p = position(lax.axis_index(axis), masks)
    chunks = value.reshape((n, value.shape[0] // n) + value.shape[1:])
    total = lax.dynamic_index_in_dim(chunks, p, keepdims=False)
    for k in range(1, n):
        send = lax.dynamic_index_in_dim(chunks, p ^ k, keepdims=False)
        total = total + lax.ppermute(send, axis, xor_perm(size, offset(k, masks)))
    return total


def gather_groups(ncol):
    bits = [1 << k for k in range(ncol.bit_length() - 1)]
    low = [m for m in bits if m < 8][::-1]
    high = [m for m in bits if m >= 8]
    groups = [tuple(low[i : i + 2]) for i in range(0, len(low), 2)]
    return groups + [tuple(high[i : i + 2]) for i in range(0, len(high), 2)]


def kept_chunk(idx, groups, nblocks):
    lo, span = 0, nblocks
    for masks in groups:
        n = 1 << len(masks)
        span //= n
        lo += span * sum(((idx & m) != 0) << b for b, m in enumerate(masks))
    return lo


def all_reduce(value, nrow, ncol):
    ndev = nrow * ncol
    bits = [1 << k for k in range(ndev.bit_length() - 1)]
    outer = tuple(ncol * m for m in (1, 2) if m < nrow)
    rest = [m for m in bits if m not in outer]
    inner = [tuple(rest[i : i + 2]) for i in range(0, len(rest), 2)]
    value = scatter_step(value, ALL, ndev, outer)
    for masks in inner:
        value = sum_step(value, ALL, ndev, masks)
    return gather_step(value, ALL, ndev, outer)


def make_body(nrow, ncol):
    assert nrow & (nrow - 1) == 0 and ncol & (ncol - 1) == 0
    row_bits = [1 << k for k in range(nrow.bit_length() - 1)]
    row_groups = [tuple(row_bits[i : i + 2]) for i in range(0, len(row_bits), 2)]
    owner_perm = [
        (r * ncol + c, c * nrow + kept_chunk(r, row_groups, nrow)) for r in range(nrow) for c in range(ncol)
    ]

    q = ncol // nrow
    z_ring = 8 if ncol % 8 == 0 and q == 4 else 0

    def col_block_of(big, small):
        if not z_ring:
            return small % q
        low = (q * big) % z_ring
        z = small % z_ring
        target = z if low <= z < low + q else (z_ring - 1 - z) % z_ring
        return target - low

    col_block_perm = []
    for big in range(nrow):
        slots = {}
        for small in range(ncol):
            j = col_block_of(big, small)
            r = slots.setdefault(j, 0)
            slots[j] = r + 1
            col_block_perm.append((big * ncol + small, r * ncol + q * big + j))
    assert sorted(d for _, d in col_block_perm) == list(range(nrow * ncol))

    def inner(trailing_adjoint, panel, panel_adjoint, diag_factor, diag_adjoint):
        r = lax.axis_index("row")
        c = lax.axis_index("col")
        inverse = lower_inverse(diag_factor)

        groups = gather_groups(ncol)
        gathered = panel
        for masks in groups:
            gathered = gather_step(gathered, "col", ncol, masks)
        order = [m for masks in groups for m in masks]
        blocks = gathered.reshape((2,) * len(order) + panel.shape)
        nbits = len(order)
        axis_of_bit = {m.bit_length() - 1: nbits - 1 - t for t, m in enumerate(order)}
        perm = [axis_of_bit[nbits - 1 - a] for a in range(nbits)] + [nbits, nbits + 1]
        gathered = blocks.transpose(perm).reshape((ncol * panel.shape[0], panel.shape[1]))

        share = lax.dot_general(
            trailing_adjoint,
            gathered,
            (((0,), (0,)), ((), ())),
            precision=lax.Precision.HIGHEST,
            preferred_element_type=jnp.float32,
        )

        span = share.shape[0]
        sends = jnp.asarray(
            [col_block_of(big, small) for big in range(nrow) for small in range(ncol)], jnp.int32
        )[r * ncol + c]
        pick = lax.dynamic_slice_in_dim(gathered, sends * span, span, 0)
        col_panel = lax.ppermute(pick, ALL, col_block_perm)

        local_term = mm(inverse.T, mm(panel_adjoint.T, panel) - 2.0 * mm(share.T, col_panel))
        rows, cols = diag_adjoint.shape
        placed = lax.dynamic_update_slice(
            jnp.zeros((rows * nrow, cols * ncol), jnp.float32), diag_adjoint, (r * rows, c * cols)
        )
        accumulated = all_reduce(placed - local_term, nrow, ncol)

        for masks in row_groups:
            share = scatter_step(share, "row", nrow, masks)
        product = lax.ppermute(share, ALL, owner_perm)
        updated = panel_adjoint - 2.0 * product
        off_adjoint = mm(updated, inverse)
        return (off_adjoint, diagonal_adjoint(diag_factor, inverse, accumulated))

    return inner


def solution(mesh):
    return jax.shard_map(
        make_body(mesh.shape["row"], mesh.shape["col"]),
        mesh=mesh,
        in_specs=(
            P("row", "col"),
            P(ALL, None),
            P(ALL, None),
            P(),
            P("row", "col"),
        ),
        out_specs=(P(ALL, None), P()),
        check_vma=False,
    )
```

```python
import jax
import jax.numpy as jnp
from jax import lax
from jax.sharding import PartitionSpec as P

ALL = ("row", "col")


def mm(a, b):
    return jnp.dot(a, b, precision=lax.Precision.HIGHEST, preferred_element_type=jnp.float32)


def lower_inverse(factor):
    n = factor.shape[0]
    index = jnp.arange(n)
    inverse = jnp.diag(1.0 / jnp.diagonal(factor))
    s = 1
    while s < n:
        inside = (index[:, None] // (2 * s)) == (index[None, :] // (2 * s))
        outside = (index[:, None] // s) != (index[None, :] // s)
        between = jnp.where(inside & outside, factor, 0.0)
        inverse = inverse - mm(mm(inverse, between), inverse)
        s *= 2
    return inverse


def diagonal_adjoint(factor, inverse, adjoint):
    product = mm(factor.T, adjoint)
    lower = jnp.tril(product) - 0.5 * jnp.diag(jnp.diag(product))
    symmetric = lower + lower.T
    half = mm(inverse.T, symmetric)
    return 0.5 * mm(half, inverse)


def xor_perm(size, mask):
    return [(i, i ^ mask) for i in range(size)]


def offset(k, masks):
    return sum(m for b, m in enumerate(masks) if (k >> b) & 1)


def position(idx, masks):
    return sum(((idx & m) != 0).astype(jnp.int32) << b for b, m in enumerate(masks))


def exchange(value, axis, size, masks):
    got = [value]
    for k in range(1, 1 << len(masks)):
        got.append(lax.ppermute(value, axis, xor_perm(size, offset(k, masks))))
    return jnp.stack(got)


def gather_step(value, axis, size, masks):
    p = position(lax.axis_index(axis), masks)
    got = exchange(value, axis, size, masks)
    return jnp.concatenate(
        [lax.dynamic_index_in_dim(got, k ^ p, keepdims=False) for k in range(1 << len(masks))], axis=0
    )


def sum_step(value, axis, size, masks):
    p = position(lax.axis_index(axis), masks)
    got = exchange(value, axis, size, masks)
    terms = [lax.dynamic_index_in_dim(got, k ^ p, keepdims=False) for k in range(1 << len(masks))]
    while len(terms) > 1:
        terms = [terms[i] + terms[i + 1] for i in range(0, len(terms), 2)]
    return terms[0]


def scatter_step(value, axis, size, masks):
    n = 1 << len(masks)
    p = position(lax.axis_index(axis), masks)
    chunks = value.reshape((n, value.shape[0] // n) + value.shape[1:])
    total = lax.dynamic_index_in_dim(chunks, p, keepdims=False)
    for k in range(1, n):
        send = lax.dynamic_index_in_dim(chunks, p ^ k, keepdims=False)
        total = total + lax.ppermute(send, axis, xor_perm(size, offset(k, masks)))
    return total


def gather_groups(ncol):
    bits = [1 << k for k in range(ncol.bit_length() - 1)]
    low = [m for m in bits if m < 8][::-1]
    high = [m for m in bits if m >= 8]
    groups = [tuple(low[i : i + 2]) for i in range(0, len(low), 2)]
    return groups + [tuple(high[i : i + 2]) for i in range(0, len(high), 2)]


def kept_chunk(idx, groups, nblocks):
    lo, span = 0, nblocks
    for masks in groups:
        n = 1 << len(masks)
        span //= n
        lo += span * sum(((idx & m) != 0) << b for b, m in enumerate(masks))
    return lo


def all_reduce(value, nrow, ncol):
    ndev = nrow * ncol
    bits = [1 << k for k in range(ndev.bit_length() - 1)]
    outer = tuple(ncol * m for m in (1, 2) if m < nrow)
    rest = [m for m in bits if m not in outer]
    inner = [tuple(rest[i : i + 2]) for i in range(0, len(rest), 2)]
    value = scatter_step(value, ALL, ndev, outer)
    for masks in inner:
        value = sum_step(value, ALL, ndev, masks)
    return gather_step(value, ALL, ndev, outer)


def make_body(nrow, ncol):
    assert nrow & (nrow - 1) == 0 and ncol & (ncol - 1) == 0
    row_bits = [1 << k for k in range(nrow.bit_length() - 1)]
    row_groups = [tuple(row_bits[i : i + 2]) for i in range(0, len(row_bits), 2)]
    owner_perm = [
        (r * ncol + c, c * nrow + kept_chunk(r, row_groups, nrow)) for r in range(nrow) for c in range(ncol)
    ]

    q = ncol // nrow
    z_ring = 8 if ncol % 8 == 0 and q == 4 else 0

    def col_block_of(big, small):
        if not z_ring:
            return small % q
        low = (q * big) % z_ring
        z = small % z_ring
        target = z if low <= z < low + q else (z_ring - 1 - z) % z_ring
        return target - low

    col_block_perm = []
    for big in range(nrow):
        slots = {}
        for small in range(ncol):
            j = col_block_of(big, small)
            r = slots.setdefault(j, 0)
            slots[j] = r + 1
            col_block_perm.append((big * ncol + small, r * ncol + q * big + j))
    assert sorted(d for _, d in col_block_perm) == list(range(nrow * ncol))

    def inner(trailing_adjoint, panel, panel_adjoint, diag_factor, diag_adjoint):
        r = lax.axis_index("row")
        c = lax.axis_index("col")
        inverse = lower_inverse(diag_factor)

        groups = gather_groups(ncol)
        gathered = panel
        rows, cols = diag_adjoint.shape
        placed = lax.dynamic_update_slice(
            jnp.zeros((rows * nrow, cols * ncol), jnp.float32), diag_adjoint, (r * rows, c * cols)
        )
        own_term = mm(panel_adjoint.T, panel)
        for step, masks in enumerate(groups):
            if step == 1:
                gathered, placed, own_term = lax.optimization_barrier((gathered, placed, own_term))
            gathered = gather_step(gathered, "col", ncol, masks)
        order = [m for masks in groups for m in masks]
        blocks = gathered.reshape((2,) * len(order) + panel.shape)
        nbits = len(order)
        axis_of_bit = {m.bit_length() - 1: nbits - 1 - t for t, m in enumerate(order)}
        perm = [axis_of_bit[nbits - 1 - a] for a in range(nbits)] + [nbits, nbits + 1]
        gathered = blocks.transpose(perm).reshape((ncol * panel.shape[0], panel.shape[1]))

        share = lax.dot_general(
            trailing_adjoint,
            gathered,
            (((0,), (0,)), ((), ())),
            precision=lax.Precision.HIGHEST,
            preferred_element_type=jnp.float32,
        )

        span = share.shape[0]
        sends = jnp.asarray(
            [col_block_of(big, small) for big in range(nrow) for small in range(ncol)], jnp.int32
        )[r * ncol + c]
        pick = lax.dynamic_slice_in_dim(gathered, sends * span, span, 0)
        col_panel = lax.ppermute(pick, ALL, col_block_perm)

        local_term = mm(inverse.T, own_term - 2.0 * mm(share.T, col_panel))
        share, reduced = lax.optimization_barrier((share, placed - local_term))
        accumulated = all_reduce(reduced, nrow, ncol)

        for masks in row_groups:
            share = scatter_step(share, "row", nrow, masks)
        product = lax.ppermute(share, ALL, owner_perm)
        updated = panel_adjoint - 2.0 * product
        off_adjoint = mm(updated, inverse)
        return (off_adjoint, diagonal_adjoint(diag_factor, inverse, accumulated))

    return inner


def solution(mesh):
    return jax.shard_map(
        make_body(mesh.shape["row"], mesh.shape["col"]),
        mesh=mesh,
        in_specs=(
            P("row", "col"),
            P(ALL, None),
            P(ALL, None),
            P(),
            P("row", "col"),
        ),
        out_specs=(P(ALL, None), P()),
        check_vma=False,
    )
```

```python
import jax
import jax.numpy as jnp
from jax import lax
from jax.sharding import PartitionSpec as P

ALL = ("row", "col")


def mm(a, b):
    return jnp.dot(a, b, precision=lax.Precision.HIGHEST, preferred_element_type=jnp.float32)


def lower_inverse(factor):
    n = factor.shape[0]
    index = jnp.arange(n)
    inverse = jnp.diag(1.0 / jnp.diagonal(factor))
    s = 1
    while s < n:
        inside = (index[:, None] // (2 * s)) == (index[None, :] // (2 * s))
        outside = (index[:, None] // s) != (index[None, :] // s)
        between = jnp.where(inside & outside, factor, 0.0)
        inverse = inverse - mm(mm(inverse, between), inverse)
        s *= 2
    return inverse


def diagonal_adjoint(factor, inverse, adjoint):
    product = mm(factor.T, adjoint)
    lower = jnp.tril(product) - 0.5 * jnp.diag(jnp.diag(product))
    symmetric = lower + lower.T
    half = mm(inverse.T, symmetric)
    return 0.5 * mm(half, inverse)


def xor_perm(size, mask):
    return [(i, i ^ mask) for i in range(size)]


def offset(k, masks):
    return sum(m for b, m in enumerate(masks) if (k >> b) & 1)


def position(idx, masks):
    return sum(((idx & m) != 0).astype(jnp.int32) << b for b, m in enumerate(masks))


def exchange(value, axis, size, masks):
    got = [value]
    for k in range(1, 1 << len(masks)):
        got.append(lax.ppermute(value, axis, xor_perm(size, offset(k, masks))))
    return jnp.stack(got)


def gather_step(value, axis, size, masks):
    p = position(lax.axis_index(axis), masks)
    got = exchange(value, axis, size, masks)
    return jnp.concatenate(
        [lax.dynamic_index_in_dim(got, k ^ p, keepdims=False) for k in range(1 << len(masks))], axis=0
    )


def sum_step(value, axis, size, masks):
    p = position(lax.axis_index(axis), masks)
    got = exchange(value, axis, size, masks)
    terms = [lax.dynamic_index_in_dim(got, k ^ p, keepdims=False) for k in range(1 << len(masks))]
    while len(terms) > 1:
        terms = [terms[i] + terms[i + 1] for i in range(0, len(terms), 2)]
    return terms[0]


def scatter_step(value, axis, size, masks):
    n = 1 << len(masks)
    p = position(lax.axis_index(axis), masks)
    chunks = value.reshape((n, value.shape[0] // n) + value.shape[1:])
    total = lax.dynamic_index_in_dim(chunks, p, keepdims=False)
    for k in range(1, n):
        send = lax.dynamic_index_in_dim(chunks, p ^ k, keepdims=False)
        total = total + lax.ppermute(send, axis, xor_perm(size, offset(k, masks)))
    return total


def gather_groups(ncol):
    bits = [1 << k for k in range(ncol.bit_length() - 1)]
    low = [m for m in bits if m < 8][::-1]
    high = [m for m in bits if m >= 8]
    groups = [tuple(low[i : i + 2]) for i in range(0, len(low), 2)]
    return groups + [tuple(high[i : i + 2]) for i in range(0, len(high), 2)]


def kept_chunk(idx, groups, nblocks):
    lo, span = 0, nblocks
    for masks in groups:
        n = 1 << len(masks)
        span //= n
        lo += span * sum(((idx & m) != 0) << b for b, m in enumerate(masks))
    return lo


def all_reduce(value, nrow, ncol):
    ndev = nrow * ncol
    bits = [1 << k for k in range(ndev.bit_length() - 1)]
    outer = tuple(ncol * m for m in (1, 2) if m < nrow)
    rest = [m for m in bits if m not in outer]
    inner = [tuple(rest[i : i + 2]) for i in range(0, len(rest), 2)]
    value = scatter_step(value, ALL, ndev, outer)
    for masks in inner:
        value = sum_step(value, ALL, ndev, masks)
    return gather_step(value, ALL, ndev, outer)


def natural(gathered, order, shape):
    nbits = len(order)
    blocks = gathered.reshape((2,) * nbits + shape)
    axis_of_bit = {m.bit_length() - 1: nbits - 1 - t for t, m in enumerate(order)}
    low = min(axis_of_bit)
    perm = [axis_of_bit[low + nbits - 1 - a] for a in range(nbits)] + [nbits, nbits + 1]
    return blocks.transpose(perm).reshape(((1 << nbits) * shape[0], shape[1]))


def make_body(nrow, ncol):
    assert nrow & (nrow - 1) == 0 and ncol & (ncol - 1) == 0
    row_bits = [1 << k for k in range(nrow.bit_length() - 1)]
    row_groups = [tuple(row_bits[i : i + 2]) for i in range(0, len(row_bits), 2)]
    owner_perm = [
        (r * ncol + c, c * nrow + kept_chunk(r, row_groups, nrow)) for r in range(nrow) for c in range(ncol)
    ]

    q = ncol // nrow
    early = ncol % 8 == 0 and q == ncol // 8 and nrow == 8
    if early:
        col_block_perm = [
            (big * ncol + small, (small % 8) * ncol + q * big + small // 8)
            for big in range(nrow)
            for small in range(ncol)
        ]
    else:
        col_block_perm = [
            (big * ncol + small, (small // q) * ncol + q * big + small % q)
            for big in range(nrow)
            for small in range(ncol)
        ]
    assert sorted(d for _, d in col_block_perm) == list(range(nrow * ncol))

    def inner(trailing_adjoint, panel, panel_adjoint, diag_factor, diag_adjoint):
        r = lax.axis_index("row")
        c = lax.axis_index("col")
        inverse = lower_inverse(diag_factor)

        groups = gather_groups(ncol)
        gathered = panel
        zsteps = [g for g in groups if all(m < 8 for m in g)]
        for step, masks in enumerate(groups):
            gathered = gather_step(gathered, "col", ncol, masks)
            if early and step == len(zsteps) - 1:
                zorder = [m for g in zsteps for m in g]
                pick = natural(gathered, zorder, panel.shape)
                col_panel = lax.ppermute(pick, ALL, col_block_perm)
        gathered = natural(gathered, [m for masks in groups for m in masks], panel.shape)

        share = lax.dot_general(
            trailing_adjoint,
            gathered,
            (((0,), (0,)), ((), ())),
            precision=lax.Precision.HIGHEST,
            preferred_element_type=jnp.float32,
        )

        span = share.shape[0]
        if not early:
            pick = lax.dynamic_slice_in_dim(gathered, (c % q) * span, span, 0)
            col_panel = lax.ppermute(pick, ALL, col_block_perm)

        local_term = mm(inverse.T, mm(panel_adjoint.T, panel) - 2.0 * mm(share.T, col_panel))
        rows, cols = diag_adjoint.shape
        placed = lax.dynamic_update_slice(
            jnp.zeros((rows * nrow, cols * ncol), jnp.float32), diag_adjoint, (r * rows, c * cols)
        )
        share, reduced = lax.optimization_barrier((share, placed - local_term))
        accumulated = all_reduce(reduced, nrow, ncol)

        for masks in row_groups:
            share = scatter_step(share, "row", nrow, masks)
        product = lax.ppermute(share, ALL, owner_perm)
        updated = panel_adjoint - 2.0 * product
        off_adjoint = mm(updated, inverse)
        return (off_adjoint, diagonal_adjoint(diag_factor, inverse, accumulated))

    return inner


def solution(mesh):
    return jax.shard_map(
        make_body(mesh.shape["row"], mesh.shape["col"]),
        mesh=mesh,
        in_specs=(
            P("row", "col"),
            P(ALL, None),
            P(ALL, None),
            P(),
            P("row", "col"),
        ),
        out_specs=(P(ALL, None), P()),
        check_vma=False,
    )
```

```python
import jax
import jax.numpy as jnp
from jax import lax
from jax.sharding import PartitionSpec as P

ALL = ("row", "col")


def mm(a, b):
    return jnp.dot(a, b, precision=lax.Precision.HIGHEST, preferred_element_type=jnp.float32)


def lower_inverse(factor):
    n = factor.shape[0]
    index = jnp.arange(n)
    inverse = jnp.diag(1.0 / jnp.diagonal(factor))
    s = 1
    while s < n:
        inside = (index[:, None] // (2 * s)) == (index[None, :] // (2 * s))
        outside = (index[:, None] // s) != (index[None, :] // s)
        between = jnp.where(inside & outside, factor, 0.0)
        inverse = inverse - mm(mm(inverse, between), inverse)
        s *= 2
    return inverse


def diagonal_adjoint(factor, inverse, adjoint):
    product = mm(factor.T, adjoint)
    lower = jnp.tril(product) - 0.5 * jnp.diag(jnp.diag(product))
    symmetric = lower + lower.T
    half = mm(inverse.T, symmetric)
    return 0.5 * mm(half, inverse)


def xor_perm(size, mask):
    return [(i, i ^ mask) for i in range(size)]


def offset(k, masks):
    return sum(m for b, m in enumerate(masks) if (k >> b) & 1)


def position(idx, masks):
    return sum(((idx & m) != 0).astype(jnp.int32) << b for b, m in enumerate(masks))


def exchange(value, axis, size, masks):
    got = [value]
    for k in range(1, 1 << len(masks)):
        got.append(lax.ppermute(value, axis, xor_perm(size, offset(k, masks))))
    return jnp.stack(got)


def gather_step(value, axis, size, masks):
    p = position(lax.axis_index(axis), masks)
    got = exchange(value, axis, size, masks)
    return jnp.concatenate(
        [lax.dynamic_index_in_dim(got, k ^ p, keepdims=False) for k in range(1 << len(masks))], axis=0
    )


def sum_step(value, axis, size, masks):
    p = position(lax.axis_index(axis), masks)
    got = exchange(value, axis, size, masks)
    terms = [lax.dynamic_index_in_dim(got, k ^ p, keepdims=False) for k in range(1 << len(masks))]
    while len(terms) > 1:
        terms = [terms[i] + terms[i + 1] for i in range(0, len(terms), 2)]
    return terms[0]


def scatter_step(value, axis, size, masks):
    n = 1 << len(masks)
    p = position(lax.axis_index(axis), masks)
    chunks = value.reshape((n, value.shape[0] // n) + value.shape[1:])
    total = lax.dynamic_index_in_dim(chunks, p, keepdims=False)
    for k in range(1, n):
        send = lax.dynamic_index_in_dim(chunks, p ^ k, keepdims=False)
        total = total + lax.ppermute(send, axis, xor_perm(size, offset(k, masks)))
    return total


def gather_groups(ncol):
    bits = [1 << k for k in range(ncol.bit_length() - 1)]
    low = [m for m in bits if m < 8][::-1]
    high = [m for m in bits if m >= 8]
    groups = [tuple(low[i : i + 2]) for i in range(0, len(low), 2)]
    return groups + [tuple(high[i : i + 2]) for i in range(0, len(high), 2)]


def kept_chunk(idx, groups, nblocks):
    lo, span = 0, nblocks
    for masks in groups:
        n = 1 << len(masks)
        span //= n
        lo += span * sum(((idx & m) != 0) << b for b, m in enumerate(masks))
    return lo


def all_reduce(value, nrow, ncol):
    ndev = nrow * ncol
    bits = [1 << k for k in range(ndev.bit_length() - 1)]
    outer = tuple(ncol * m for m in (1, 2) if m < nrow)
    rest = [m for m in bits if m not in outer]
    inner = [tuple(rest[i : i + 2]) for i in range(0, len(rest), 2)]
    value = scatter_step(value, ALL, ndev, outer)
    for masks in inner:
        value = sum_step(value, ALL, ndev, masks)
    return gather_step(value, ALL, ndev, outer)


def make_body(nrow, ncol):
    assert nrow & (nrow - 1) == 0 and ncol & (ncol - 1) == 0
    row_bits = [1 << k for k in range(nrow.bit_length() - 1)]
    row_groups = [(m,) for m in row_bits]
    owner_perm = [
        (r * ncol + c, c * nrow + kept_chunk(r, row_groups, nrow)) for r in range(nrow) for c in range(ncol)
    ]

    q = ncol // nrow
    z_ring = 8 if ncol % 8 == 0 and q == 4 else 0

    def col_block_of(big, small):
        if not z_ring:
            return small % q
        low = (q * big) % z_ring
        z = small % z_ring
        target = z if low <= z < low + q else (z_ring - 1 - z) % z_ring
        return target - low

    col_block_perm = []
    for big in range(nrow):
        slots = {}
        for small in range(ncol):
            j = col_block_of(big, small)
            r = slots.setdefault(j, 0)
            slots[j] = r + 1
            col_block_perm.append((big * ncol + small, r * ncol + q * big + j))
    assert sorted(d for _, d in col_block_perm) == list(range(nrow * ncol))

    def inner(trailing_adjoint, panel, panel_adjoint, diag_factor, diag_adjoint):
        r = lax.axis_index("row")
        c = lax.axis_index("col")
        inverse = lower_inverse(diag_factor)

        groups = gather_groups(ncol)
        gathered = panel
        for masks in groups:
            gathered = gather_step(gathered, "col", ncol, masks)
        order = [m for masks in groups for m in masks]
        blocks = gathered.reshape((2,) * len(order) + panel.shape)
        nbits = len(order)
        axis_of_bit = {m.bit_length() - 1: nbits - 1 - t for t, m in enumerate(order)}
        perm = [axis_of_bit[nbits - 1 - a] for a in range(nbits)] + [nbits, nbits + 1]
        gathered = blocks.transpose(perm).reshape((ncol * panel.shape[0], panel.shape[1]))

        share = lax.dot_general(
            trailing_adjoint,
            gathered,
            (((0,), (0,)), ((), ())),
            precision=lax.Precision.HIGHEST,
            preferred_element_type=jnp.float32,
        )

        span = share.shape[0]
        sends = jnp.asarray(
            [col_block_of(big, small) for big in range(nrow) for small in range(ncol)], jnp.int32
        )[r * ncol + c]
        pick = lax.dynamic_slice_in_dim(gathered, sends * span, span, 0)
        col_panel = lax.ppermute(pick, ALL, col_block_perm)

        local_term = mm(inverse.T, mm(panel_adjoint.T, panel) - 2.0 * mm(share.T, col_panel))
        rows, cols = diag_adjoint.shape
        placed = lax.dynamic_update_slice(
            jnp.zeros((rows * nrow, cols * ncol), jnp.float32), diag_adjoint, (r * rows, c * cols)
        )
        share, reduced = lax.optimization_barrier((share, placed - local_term))
        accumulated = all_reduce(reduced, nrow, ncol)

        for masks in row_groups:
            share = scatter_step(share, "row", nrow, masks)
        product = lax.ppermute(share, ALL, owner_perm)
        updated = panel_adjoint - 2.0 * product
        off_adjoint = mm(updated, inverse)
        return (off_adjoint, diagonal_adjoint(diag_factor, inverse, accumulated))

    return inner


def solution(mesh):
    return jax.shard_map(
        make_body(mesh.shape["row"], mesh.shape["col"]),
        mesh=mesh,
        in_specs=(
            P("row", "col"),
            P(ALL, None),
            P(ALL, None),
            P(),
            P("row", "col"),
        ),
        out_specs=(P(ALL, None), P()),
        check_vma=False,
    )
```
